256 devices in a mesh: chan: 32 (over z, x_lo, core), win: 8 (over x_hi, y).
Axes of the slice: x: 4 (x_hi: 2, x_lo: 2; x = x_hi * 2 + x_lo), y: 4, z: 8, core: 2. Of those that a mesh axis runs over, the one named last changes fastest.
Arguments:
- strain_rate: bfloat16 [8, 1024, 8192], P('win', 'chan'), may hold values from -600 to 600
- bandpass_taps: bfloat16 [65], replicated, may hold values from -0.75 to 0.75
- pair_offsets: int32 [32, 6], P('chan'), may hold values from -1 to 31, as said below
- lag_limit: int32 [32, 6], P('chan'), may hold values from 1 to 8
Outputs:
- correlations: float32 [6, 8192, 2176], P(None, ('chan', 'win'))
The draws below stay inside these ranges and needn't reach their ends.
Inputs may be any that keep to these rules, and one draw needn't show every extreme that they name: `pair_offsets`: row b lists distinct block offsets o (partner block (b + o) mod 32) in its first slots and -1 in the remaining slots; every row has at least one offset, some row uses all 6 slots and some row only one.
All inputs are finite; a program needn't handle non-finite values.
Results may differ from the reference program's by a relative error of at most 0.0027.
Values may be sent and summed in bfloat16 or wider, within the bound.
No kernel may reach another device: no remote copies, remote signals or barrier semaphores. Data moves between devices by JAX's collectives and lax.ppermute only.
A program may use at most 128 MiB of HBM per device.

```python
import math
import jax
import jax.numpy as jnp
from jax import lax

CHANNELS = 8192
NBLOCKS = 32
VIRTUAL_SOURCES = 128
SEGMENT_LENGTH = 1024
HALF = 32
MAXIMUM_LAG = 8
SLOTS = 6
N_CHAN = 32
N_WIN = 8


def draw_strain_rate(key, part):
    sensor_scaling_seed, transient_seed, ambient_random_seed = jax.random.split(key, 3)
    channel_gain = jnp.exp(jax.random.uniform(sensor_scaling_seed, (CHANNELS,), jnp.float32, 0.0, math.log(10.0)))
    transient_spikes = jnp.exp(jax.random.uniform(transient_seed, (N_WIN, SEGMENT_LENGTH // 32), jnp.float32, 0.0, math.log(10.0)))
    smooth_magnitude_curve = jnp.repeat(transient_spikes, 32, axis=1)
    noise_field = jax.random.truncated_normal(ambient_random_seed, -6.0, 6.0, (N_WIN, SEGMENT_LENGTH, CHANNELS), jnp.float32)
    return (noise_field * smooth_magnitude_curve[:, :, None] * channel_gain[None, None, :]).astype(jnp.bfloat16)


def draw_pair_offsets(key, part):
    key_score, key_full, key_single, key_busy, key_few = jax.random.split(key, 5)
    row_ids = jnp.arange(NBLOCKS, dtype=jnp.int32)
    scores = jax.random.randint(key_score, (NBLOCKS, NBLOCKS), 0, 2 ** 20, jnp.int32) * NBLOCKS + row_ids[None, :]
    full_row = jax.random.randint(key_full, (), 0, NBLOCKS, jnp.int32)
    single = (full_row + 1 + jax.random.randint(key_single, (), 0, NBLOCKS - 1, jnp.int32)) % NBLOCKS
    last_column = row_ids == NBLOCKS - 1
    scores = jnp.where((row_ids[:, None] == full_row) & last_column[None, :], -1, scores)
    ranked = jnp.argsort(scores, axis=1, stable=True)[:, :SLOTS].astype(jnp.int32)
    busy_rows = jax.random.randint(key_busy, (NBLOCKS,), 0, 4, jnp.int32) == 0
    few_slots = jax.random.randint(key_few, (NBLOCKS,), 1, 3, jnp.int32)
    used_slots = jnp.where(busy_rows, SLOTS, few_slots)
    used_slots = jnp.where(row_ids == full_row, SLOTS, used_slots)
    used_slots = jnp.where(row_ids == single, 1, used_slots)
    slot_ids = jnp.arange(SLOTS, dtype=jnp.int32)
    return jnp.where(slot_ids[None, :] < used_slots[:, None], ranked, -1).astype(jnp.int32)


def set_ends(array, own_key, low, top_value):
    extent = array.shape
    spot = [jax.random.randint(jax.random.fold_in(own_key, axis), (), 0, extent[axis]) for axis in range(len(extent))]
    array = array.at[tuple(spot)].set(low)
    longest = extent.index(max(extent))
    spot[longest] = (spot[longest] + 1) % extent[longest]
    return array.at[tuple(spot)].set(top_value)


def centred(key, extent, width, limit, held_as=jnp.bfloat16):
    values = width * jax.random.normal(key, extent, jnp.float32)
    return jnp.clip(values, min=-limit, max=limit).astype(held_as)


def setup_inputs(seed: int = 0) -> dict:
    keys = jax.random.split(jax.random.key(seed), 5)
    return {
        "strain_rate": draw_strain_rate(jax.random.fold_in(keys[4], 71), 0),
        "bandpass_taps": centred(keys[1], (2 * HALF + 1,), (2 * HALF + 1) ** -0.5, 0.75),
        "pair_offsets": draw_pair_offsets(jax.random.fold_in(keys[4], 71), 0),
        "lag_limit": set_ends(jax.random.randint(keys[3], (NBLOCKS, SLOTS), 1, MAXIMUM_LAG + 1), jax.random.fold_in(keys[3], 1), 1, MAXIMUM_LAG).astype(jnp.int32),
    }


def band_filter(values, taps):
    samples, channel_count = values.shape
    tap_count = taps.shape[0]
    half_width = (tap_count - 1) // 2
    block_len = min(256, samples)
    pieces = samples // block_len
    padded = jnp.pad(values, ((half_width, half_width), (0, 0)))
    head_rows = padded[:samples].reshape(pieces, block_len, channel_count)
    rest_rows = jnp.pad(padded[block_len:], ((0, block_len - 2 * half_width), (0, 0)))
    tail_rows = rest_rows.reshape(pieces, block_len, channel_count)[:, :2 * half_width]
    window = jnp.concatenate([head_rows, tail_rows], axis=1)
    period = jnp.concatenate([taps, jnp.zeros((block_len,), taps.dtype)])
    matrix = jnp.tile(period, block_len)[:block_len * (block_len + 2 * half_width)]
    matrix = matrix.reshape(block_len, block_len + 2 * half_width)
    filtered = jnp.einsum('ij,bjc->bic', matrix.astype(jnp.float32), window.astype(jnp.float32), precision=lax.Precision.HIGHEST)
    return filtered.reshape(samples, channel_count)

def normalize(window, taps):
    filtered = band_filter(window, taps)
    tap_count = taps.shape[0]
    magnitude = lax.optimization_barrier(jnp.abs(filtered).astype(jnp.bfloat16))
    box_taps = jnp.ones((tap_count,), jnp.bfloat16)
    mean_level = band_filter(magnitude, box_taps) * (1.0 / tap_count)
    return (filtered / (mean_level + 1e-05)).astype(jnp.bfloat16)

def lagged(source_traces, samples):
    padded = jnp.pad(source_traces, ((0, 0), (0, 0), (MAXIMUM_LAG, MAXIMUM_LAG)))
    lag_rows = [padded[:, :, lag_index:lag_index + samples] for lag_index in range(2 * MAXIMUM_LAG + 1)]
    return jnp.concatenate(lag_rows, axis=1)

def reference(strain_rate, bandpass_taps, pair_offsets, lag_limit):
    blocks = N_CHAN
    channel_count = CHANNELS // blocks
    source_spacing = channel_count // VIRTUAL_SOURCES
    column_list = (2 * MAXIMUM_LAG + 1) * VIRTUAL_SOURCES
    cleaned = lax.map(lambda window: normalize(window, bandpass_taps), strain_rate)
    source_channels = jnp.swapaxes(cleaned[:, :, ::source_spacing], 1, 2)
    lag_samples = jnp.arange(column_list, dtype=jnp.int32) // VIRTUAL_SOURCES - MAXIMUM_LAG

    def per_block(block_id):
        receivers = lax.dynamic_slice_in_dim(cleaned, block_id * channel_count, channel_count, 2).astype(jnp.float32)
        results = []
        for slot_index in range(SLOTS):
            offset_now = pair_offsets[block_id, slot_index]
            limit_now = lag_limit[block_id, slot_index]

            def compute(unused):
                paired_block = ((block_id + offset_now) % blocks).astype(jnp.int32)
                source_traces = lax.dynamic_slice_in_dim(source_channels, (paired_block * VIRTUAL_SOURCES).astype(jnp.int32), VIRTUAL_SOURCES, 1)
                stacked = lagged(source_traces, SEGMENT_LENGTH).astype(receivers.dtype)
                product = jnp.einsum('wtr,wct->rc', receivers, stacked, precision=lax.Precision.HIGHEST)
                lag_mask = (jnp.abs(lag_samples) <= limit_now).astype(receivers.dtype)
                return product * lag_mask[None, :]

            def nothing(unused):
                return jnp.zeros((channel_count, column_list), receivers.dtype)
            results.append(lax.cond(offset_now >= 0, compute, nothing, 0))
        return jnp.stack(results)
    result = lax.map(per_block, jnp.arange(blocks, dtype=jnp.int32))
    factor = 1.0 / math.sqrt(SEGMENT_LENGTH * N_WIN)
    return jnp.transpose(result, (1, 0, 2, 3)).reshape(SLOTS, CHANNELS, column_list) * factor
```

```python
import math

import jax
import jax.numpy as jnp
from jax import lax
from jax.sharding import PartitionSpec as P

VIRTUAL_SOURCES = 128
MAXIMUM_LAG = 8


def band_filter(values, taps):
    samples, channel_count = values.shape
    tap_count = taps.shape[0]
    half_width = (tap_count - 1) // 2
    block_len = min(256, samples)
    pieces = samples // block_len
    padded = jnp.pad(values, ((half_width, half_width), (0, 0)))
    head_rows = padded[:samples].reshape(pieces, block_len, channel_count)
    rest_rows = jnp.pad(padded[block_len:], ((0, block_len - 2 * half_width), (0, 0)))
    tail_rows = rest_rows.reshape(pieces, block_len, channel_count)[:, : 2 * half_width]
    window = jnp.concatenate([head_rows, tail_rows], axis=1)
    period = jnp.concatenate([taps, jnp.zeros((block_len,), taps.dtype)])
    matrix = jnp.tile(period, block_len)[: block_len * (block_len + 2 * half_width)]
    matrix = matrix.reshape(block_len, block_len + 2 * half_width)
    filtered = jnp.einsum("ij,bjc->bic", matrix, window, preferred_element_type=jnp.float32)
    return filtered.reshape(samples, channel_count)


def normalize(window, taps):
    filtered = band_filter(window, taps)
    tap_count = taps.shape[0]
    magnitude = jnp.abs(filtered).astype(jnp.bfloat16)
    box_taps = jnp.ones((tap_count,), jnp.bfloat16)
    mean_level = band_filter(magnitude, box_taps) * (1.0 / tap_count)
    return (filtered / (mean_level + 1e-05)).astype(jnp.bfloat16)


def on_device(strain_rate, bandpass_taps, pair_offsets, lag_limit):
    n_chan = lax.axis_size("chan")
    n_win = lax.axis_size("win")
    _, piece, channels = strain_rate.shape
    channel_count = channels // n_chan
    spacing = channel_count // VIRTUAL_SOURCES
    group = VIRTUAL_SOURCES // n_win
    rows = channel_count // n_win
    lags = 2 * MAXIMUM_LAG + 1

    blocks_first = jnp.transpose(strain_rate[0].reshape(piece, n_chan, channel_count), (1, 0, 2))
    gathered = lax.all_to_all(blocks_first, "chan", 0, 0, tiled=True)
    receivers = normalize(gathered.reshape(n_chan * piece, channel_count), bandpass_taps)
    samples = receivers.shape[0]

    sources = jnp.transpose(receivers[:, ::spacing]).reshape(n_win, group, samples)
    sources = lax.all_to_all(sources, "win", 0, 0, tiled=True)
    panels = lax.all_gather(sources, "chan", axis=0, tiled=False)
    stack = lax.all_gather(receivers, "win", axis=0, tiled=False)

    block = lax.axis_index("chan")
    offsets = pair_offsets[0]
    limits = lag_limit[0]
    lag_of_column = jnp.repeat(jnp.arange(lags, dtype=jnp.int32) - MAXIMUM_LAG, group)

    def slot(k):
        offset_now = offsets[k]

        def compute(unused):
            partner = lax.rem(block + offset_now, n_chan)
            traces = lax.dynamic_index_in_dim(panels, partner, 0, keepdims=False)
            padded = jnp.pad(traces, ((0, 0), (0, 0), (MAXIMUM_LAG, MAXIMUM_LAG)))
            lagged = jnp.concatenate(
                [padded[:, None, :, i : i + samples] for i in range(lags)], axis=1
            ).reshape(n_win, lags * group, samples)
            product = jnp.einsum("wtr,wct->rc", stack, lagged, preferred_element_type=jnp.float32)
            mask = (jnp.abs(lag_of_column) <= limits[k]).astype(jnp.float32)
            return product * mask[None, :]

        def nothing(unused):
            return jnp.zeros((channel_count, lags * group), jnp.float32)

        return lax.cond(offset_now >= 0, compute, nothing, 0)

    result = jnp.stack([slot(k) for k in range(offsets.shape[0])])
    factor = 1.0 / math.sqrt(samples * n_win)
    result = result * factor
    slots = result.shape[0]
    result = result.reshape(slots, n_win, rows, lags * group)
    result = lax.all_to_all(result, "win", 1, 1, tiled=True)
    result = result.reshape(slots, n_win, rows, lags, group)
    result = jnp.transpose(result, (0, 2, 3, 1, 4))
    return result.reshape(slots, rows, lags * VIRTUAL_SOURCES)


def solution(mesh):
    placed = (P("win", "chan", None), P(), P("chan", None), P("chan", None))
    return jax.shard_map(
        on_device,
        mesh=mesh,
        in_specs=placed,
        out_specs=P(None, ("chan", "win"), None),
        check_vma=False,
    )
```

```python
import math

import jax
import jax.numpy as jnp
from jax import lax
from jax.sharding import PartitionSpec as P

VIRTUAL_SOURCES = 128
MAXIMUM_LAG = 8


def shifted(block, axis, distance):
    devices = range(lax.axis_size(axis))
    route = [(i, (i + distance) % len(devices)) for i in devices]
    return lax.ppermute(block, axis, route)


def band_filter(values, taps):
    samples, channel_count = values.shape
    tap_count = taps.shape[0]
    half_width = (tap_count - 1) // 2
    block_len = min(256, samples)
    pieces = samples // block_len
    padded = jnp.pad(values, ((half_width, half_width), (0, 0)))
    head_rows = padded[:samples].reshape(pieces, block_len, channel_count)
    rest_rows = jnp.pad(padded[block_len:], ((0, block_len - 2 * half_width), (0, 0)))
    tail_rows = rest_rows.reshape(pieces, block_len, channel_count)[:, : 2 * half_width]
    window = jnp.concatenate([head_rows, tail_rows], axis=1)
    period = jnp.concatenate([taps, jnp.zeros((block_len,), taps.dtype)])
    matrix = jnp.tile(period, block_len)[: block_len * (block_len + 2 * half_width)]
    matrix = matrix.reshape(block_len, block_len + 2 * half_width)
    filtered = jnp.einsum("ij,bjc->bic", matrix, window, preferred_element_type=jnp.float32)
    return filtered.reshape(samples, channel_count)


def normalize(window, taps):
    filtered = band_filter(window, taps)
    tap_count = taps.shape[0]
    magnitude = jnp.abs(filtered).astype(jnp.bfloat16)
    box_taps = jnp.ones((tap_count,), jnp.bfloat16)
    mean_level = band_filter(magnitude, box_taps) * (1.0 / tap_count)
    return (filtered / (mean_level + 1e-05)).astype(jnp.bfloat16)


def on_device(strain_rate, bandpass_taps, pair_offsets, lag_limit):
    n_chan = lax.axis_size("chan")
    n_win = lax.axis_size("win")
    _, piece, channels = strain_rate.shape
    channel_count = channels // n_chan
    spacing = channel_count // VIRTUAL_SOURCES
    group = VIRTUAL_SOURCES // n_win
    rows = channel_count // n_win
    lags = 2 * MAXIMUM_LAG + 1

    blocks_first = jnp.transpose(strain_rate[0].reshape(piece, n_chan, channel_count), (1, 0, 2))
    gathered = lax.all_to_all(blocks_first, "chan", 0, 0, tiled=True)
    receivers = normalize(gathered.reshape(n_chan * piece, channel_count), bandpass_taps)
    samples = receivers.shape[0]

    me = lax.axis_index("win")
    sources = jnp.transpose(receivers[:, ::spacing]).reshape(n_win, group, samples)
    source_pieces = [lax.dynamic_index_in_dim(sources, me, 0, keepdims=False)]
    receiver_pieces = [receivers]
    for distance in range(1, n_win):
        target = lax.rem(me + distance, n_win)
        source_pieces.append(
            shifted(lax.dynamic_index_in_dim(sources, target, 0, keepdims=False), "win", distance)
        )
        receiver_pieces.append(shifted(receivers, "win", distance))
    panels = lax.all_gather(jnp.stack(source_pieces), "chan", axis=0, tiled=False)
    stack = jnp.stack(receiver_pieces)

    block = lax.axis_index("chan")
    offsets = pair_offsets[0]
    limits = lag_limit[0]
    lag_of_column = jnp.repeat(jnp.arange(lags, dtype=jnp.int32) - MAXIMUM_LAG, group)

    def slot(settings):
        offset_now, limit_now = settings

        def compute(unused):
            partner = lax.rem(block + offset_now, n_chan)
            traces = lax.dynamic_index_in_dim(panels, partner, 0, keepdims=False)
            padded = jnp.pad(traces, ((0, 0), (0, 0), (MAXIMUM_LAG, MAXIMUM_LAG)))
            lagged = jnp.concatenate(
                [padded[:, None, :, i : i + samples] for i in range(lags)], axis=1
            ).reshape(n_win, lags * group, samples)
            product = jnp.einsum("wtr,wct->rc", stack, lagged, preferred_element_type=jnp.float32)
            mask = (jnp.abs(lag_of_column) <= limit_now).astype(jnp.float32)
            return product * mask[None, :]

        def nothing(unused):
            return jnp.zeros((channel_count, lags * group), jnp.float32)

        return lax.cond(offset_now >= 0, compute, nothing, 0)

    result = lax.map(slot, (offsets, limits))
    factor = 1.0 / math.sqrt(samples * n_win)
    result = result * factor
    slots = result.shape[0]
    result = jnp.transpose(result.reshape(slots, n_win, rows, lags * group), (1, 0, 2, 3))
    result = lax.all_to_all(result, "win", 0, 0, tiled=True)
    result = result.reshape(n_win, slots, rows, lags, group)
    result = jnp.transpose(result, (1, 2, 3, 0, 4))
    return result.reshape(slots, rows, lags * VIRTUAL_SOURCES)


def solution(mesh):
    placed = (P("win", "chan", None), P(), P("chan", None), P("chan", None))
    return jax.shard_map(
        on_device,
        mesh=mesh,
        in_specs=placed,
        out_specs=P(None, ("chan", "win"), None),
        check_vma=False,
    )
```

```python
import math

import jax
import jax.numpy as jnp
from jax import lax
from jax.sharding import PartitionSpec as P

VIRTUAL_SOURCES = 128
MAXIMUM_LAG = 8


def shifted(block, axis, distance):
    devices = range(lax.axis_size(axis))
    route = [(i, (i + distance) % len(devices)) for i in devices]
    return lax.ppermute(block, axis, route)


def band_filter(values, taps):
    samples, channel_count = values.shape
    tap_count = taps.shape[0]
    half_width = (tap_count - 1) // 2
    block_len = min(256, samples)
    pieces = samples // block_len
    padded = jnp.pad(values, ((half_width, half_width), (0, 0)))
    head_rows = padded[:samples].reshape(pieces, block_len, channel_count)
    rest_rows = jnp.pad(padded[block_len:], ((0, block_len - 2 * half_width), (0, 0)))
    tail_rows = rest_rows.reshape(pieces, block_len, channel_count)[:, : 2 * half_width]
    window = jnp.concatenate([head_rows, tail_rows], axis=1)
    period = jnp.concatenate([taps, jnp.zeros((block_len,), taps.dtype)])
    matrix = jnp.tile(period, block_len)[: block_len * (block_len + 2 * half_width)]
    matrix = matrix.reshape(block_len, block_len + 2 * half_width)
    filtered = jnp.einsum("ij,bjc->bic", matrix, window, preferred_element_type=jnp.float32)
    return filtered.reshape(samples, channel_count)


def normalize(window, taps):
    filtered = band_filter(window, taps)
    tap_count = taps.shape[0]
    magnitude = jnp.abs(filtered).astype(jnp.bfloat16)
    box_taps = jnp.ones((tap_count,), jnp.bfloat16)
    mean_level = band_filter(magnitude, box_taps) * (1.0 / tap_count)
    return (filtered / (mean_level + 1e-05)).astype(jnp.bfloat16)


def on_device(strain_rate, bandpass_taps, pair_offsets, lag_limit):
    n_chan = lax.axis_size("chan")
    n_win = lax.axis_size("win")
    _, piece, channels = strain_rate.shape
    channel_count = channels // n_chan
    spacing = channel_count // VIRTUAL_SOURCES
    group = VIRTUAL_SOURCES // n_win
    rows = channel_count // n_win
    lags = 2 * MAXIMUM_LAG + 1

    blocks_first = jnp.transpose(strain_rate[0].reshape(piece, n_chan, channel_count), (1, 0, 2))
    gathered = lax.all_to_all(blocks_first, "chan", 0, 0, tiled=True)
    receivers = normalize(gathered.reshape(n_chan * piece, channel_count), bandpass_taps)
    samples = receivers.shape[0]

    me = lax.axis_index("win")
    sources = jnp.transpose(receivers[:, ::spacing]).reshape(n_win, group, samples)
    source_pieces = [lax.dynamic_index_in_dim(sources, me, 0, keepdims=False)]
    receiver_pieces = [receivers]
    for distance in range(1, n_win):
        target = lax.rem(me + distance, n_win)
        source_pieces.append(
            shifted(lax.dynamic_index_in_dim(sources, target, 0, keepdims=False), "win", distance)
        )
        receiver_pieces.append(shifted(receivers, "win", distance))
    panels = lax.all_gather(jnp.stack(source_pieces), "chan", axis=0, tiled=False)
    stack = jnp.stack(receiver_pieces)

    block = lax.axis_index("chan")
    offsets = pair_offsets[0]
    limits = lag_limit[0]
    slots = offsets.shape[0]

    partners = lax.rem(block + offsets + n_chan, n_chan)
    chosen = jnp.take(panels, partners, axis=0)
    padded = jnp.pad(chosen, ((0, 0), (0, 0), (0, 0), (MAXIMUM_LAG, MAXIMUM_LAG)))
    columns = []
    for w in range(n_win):
        lag_rows = jnp.stack([padded[:, w, :, i : i + samples] for i in range(lags)], axis=1)
        columns.append(lag_rows.reshape(slots * lags * group, samples))
    lagged = jnp.concatenate(columns, axis=1)
    product = lax.dot_general(
        lagged,
        stack.reshape(n_win * samples, channel_count),
        (((1,), (0,)), ((), ())),
        preferred_element_type=jnp.float32,
    )
    lag_ids = jnp.arange(lags, dtype=jnp.int32) - MAXIMUM_LAG
    kept = (jnp.abs(lag_ids)[None, :] <= limits[:, None]) & (offsets >= 0)[:, None]
    factor = 1.0 / math.sqrt(samples * n_win)
    weights = jnp.repeat(kept.astype(jnp.float32).reshape(slots * lags), group) * factor
    result = jnp.transpose(product * weights[:, None]).reshape(n_win, rows, slots * lags * group)
    result = lax.all_to_all(result, "win", 0, 0, tiled=True)
    result = result.reshape(n_win, rows, slots, lags, group)
    result = jnp.transpose(result, (2, 1, 3, 0, 4))
    return result.reshape(slots, rows, lags * VIRTUAL_SOURCES)


def solution(mesh):
    placed = (P("win", "chan", None), P(), P("chan", None), P("chan", None))
    return jax.shard_map(
        on_device,
        mesh=mesh,
        in_specs=placed,
        out_specs=P(None, ("chan", "win"), None),
        check_vma=False,
    )
```

```python
import math

import jax
import jax.numpy as jnp
from jax import lax
from jax.sharding import PartitionSpec as P


VIRTUAL_SOURCES = 128
MAXIMUM_LAG = 8


def shifted(block, axis, distance):
    devices = range(lax.axis_size(axis))
    route = [(i, (i + distance) % len(devices)) for i in devices]
    return lax.ppermute(block, axis, route)


def band_filter(values, taps):
    samples, channel_count = values.shape
    tap_count = taps.shape[0]
    half_width = (tap_count - 1) // 2
    block_len = min(256, samples)
    pieces = samples // block_len
    padded = jnp.pad(values, ((half_width, half_width), (0, 0)))
    head_rows = padded[:samples].reshape(pieces, block_len, channel_count)
    rest_rows = jnp.pad(padded[block_len:], ((0, block_len - 2 * half_width), (0, 0)))
    tail_rows = rest_rows.reshape(pieces, block_len, channel_count)[:, : 2 * half_width]
    window = jnp.concatenate([head_rows, tail_rows], axis=1)
    period = jnp.concatenate([taps, jnp.zeros((block_len,), taps.dtype)])
    matrix = jnp.tile(period, block_len)[: block_len * (block_len + 2 * half_width)]
    matrix = matrix.reshape(block_len, block_len + 2 * half_width)
    filtered = jnp.einsum("ij,bjc->bic", matrix, window, preferred_element_type=jnp.float32)
    return filtered.reshape(samples, channel_count)


def normalize(window, taps):
    filtered = band_filter(window, taps)
    tap_count = taps.shape[0]
    magnitude = jnp.abs(filtered).astype(jnp.bfloat16)
    box_taps = jnp.ones((tap_count,), jnp.bfloat16)
    mean_level = band_filter(magnitude, box_taps) * (1.0 / tap_count)
    return (filtered / (mean_level + 1e-05)).astype(jnp.bfloat16)


def on_device(strain_rate, bandpass_taps, pair_offsets, lag_limit):
    n_chan = lax.axis_size("chan")
    n_win = lax.axis_size("win")
    _, piece, channels = strain_rate.shape
    channel_count = channels // n_chan
    spacing = channel_count // VIRTUAL_SOURCES
    group = VIRTUAL_SOURCES // n_win
    rows = channel_count // n_win
    lags = 2 * MAXIMUM_LAG + 1

    blocks_first = jnp.transpose(strain_rate[0].reshape(piece, n_chan, channel_count), (1, 0, 2))
    gathered = lax.all_to_all(blocks_first, "chan", 0, 0, tiled=True)
    receivers = normalize(gathered.reshape(n_chan * piece, channel_count), bandpass_taps)
    samples = receivers.shape[0]

    me = lax.axis_index("win")
    pick = (
        jnp.arange(channel_count, dtype=jnp.int32)[None, :]
        == spacing * jnp.arange(VIRTUAL_SOURCES, dtype=jnp.int32)[:, None]
    ).astype(receivers.dtype)
    sources = lax.dot_general(
        pick, receivers, (((1,), (1,)), ((), ())), preferred_element_type=jnp.float32
    ).astype(receivers.dtype).reshape(n_win, group, samples)
    source_pieces = [lax.dynamic_index_in_dim(sources, me, 0, keepdims=False)]
    receiver_pieces = [receivers]
    for distance in range(1, n_win):
        target = lax.rem(me + distance, n_win)
        source_pieces.append(
            shifted(lax.dynamic_index_in_dim(sources, target, 0, keepdims=False), "win", distance)
        )
        receiver_pieces.append(shifted(receivers, "win", distance))
    stack = jnp.stack(receiver_pieces)

    block = lax.axis_index("chan")
    offsets = pair_offsets[0]
    limits = lag_limit[0]
    slots = offsets.shape[0]

    partners = lax.rem(block + offsets + n_chan, n_chan)
    half = n_win // 2
    product = None
    for first in (0, half):
        panels = lax.all_gather(
            jnp.stack(source_pieces[first : first + half]), "chan", axis=0, tiled=False
        )
        if product is not None:
            panels, product = lax.optimization_barrier((panels, product))
        chosen = jnp.take(panels, partners, axis=0, mode="clip")
        padded = jnp.pad(chosen, ((0, 0), (0, 0), (0, 0), (MAXIMUM_LAG, MAXIMUM_LAG)))
        columns = []
        for w in range(half):
            lag_rows = jnp.stack([padded[:, w, :, i : i + samples] for i in range(lags)], axis=1)
            columns.append(lag_rows.reshape(slots * lags * group, samples))
        lagged = jnp.concatenate(columns, axis=1)
        partial = lax.dot_general(
            lagged,
            stack[first : first + half].reshape(half * samples, channel_count),
            (((1,), (0,)), ((), ())),
            preferred_element_type=jnp.float32,
        )
        product = partial if product is None else product + partial
    lag_ids = jnp.arange(lags, dtype=jnp.int32) - MAXIMUM_LAG
    kept = (jnp.abs(lag_ids)[None, :] <= limits[:, None]) & (offsets >= 0)[:, None]
    factor = 1.0 / math.sqrt(samples * n_win)
    weights = jnp.repeat(kept.astype(jnp.float32).reshape(slots * lags), group) * factor
    result = jnp.transpose(product * weights[:, None]).reshape(n_win, rows, slots * lags * group)
    result = lax.all_to_all(result, "win", 0, 0, tiled=True)
    result = result.reshape(n_win, rows, slots, lags, group)
    result = jnp.transpose(result, (2, 1, 3, 0, 4))
    return result.reshape(slots, rows, lags * VIRTUAL_SOURCES)


def solution(mesh):
    placed = (P("win", "chan", None), P(), P("chan", None), P("chan", None))
    return jax.shard_map(
        on_device,
        mesh=mesh,
        in_specs=placed,
        out_specs=P(None, ("chan", "win"), None),
        check_vma=False,
    )
```

```python
import math

import jax
import jax.numpy as jnp
from jax import lax
from jax.sharding import Mesh, PartitionSpec as P


VIRTUAL_SOURCES = 128
MAXIMUM_LAG = 8


def shifted(block, axis, distance):
    devices = range(lax.axis_size(axis))
    route = [(i, (i + distance) % len(devices)) for i in devices]
    return lax.ppermute(block, axis, route)


def band_filter(values, taps):
    samples, channel_count = values.shape
    tap_count = taps.shape[0]
    half_width = (tap_count - 1) // 2
    block_len = min(256, samples)
    pieces = samples // block_len
    padded = jnp.pad(values, ((half_width, half_width), (0, 0)))
    head_rows = padded[:samples].reshape(pieces, block_len, channel_count)
    rest_rows = jnp.pad(padded[block_len:], ((0, block_len - 2 * half_width), (0, 0)))
    tail_rows = rest_rows.reshape(pieces, block_len, channel_count)[:, : 2 * half_width]
    window = jnp.concatenate([head_rows, tail_rows], axis=1)
    period = jnp.concatenate([taps, jnp.zeros((block_len,), taps.dtype)])
    matrix = jnp.tile(period, block_len)[: block_len * (block_len + 2 * half_width)]
    matrix = matrix.reshape(block_len, block_len + 2 * half_width)
    filtered = jnp.einsum("ij,bjc->bic", matrix, window, preferred_element_type=jnp.float32)
    return filtered.reshape(samples, channel_count)


def normalize(window, taps):
    filtered = band_filter(window, taps)
    tap_count = taps.shape[0]
    magnitude = jnp.abs(filtered).astype(jnp.bfloat16)
    box_taps = jnp.ones((tap_count,), jnp.bfloat16)
    mean_level = band_filter(magnitude, box_taps) * (1.0 / tap_count)
    return (filtered / (mean_level + 1e-05)).astype(jnp.bfloat16)


def on_device(strain_rate, bandpass_taps, pair_offsets, lag_limit):
    blocks_axis = ("chips", "core")
    n_chips = lax.axis_size("chips")
    n_core = lax.axis_size("core")
    n_chan = n_chips * n_core
    n_win = lax.axis_size("win")
    _, piece, channels = strain_rate.shape
    channel_count = channels // n_chan
    spacing = channel_count // VIRTUAL_SOURCES
    group = VIRTUAL_SOURCES // n_win
    rows = channel_count // n_win
    lags = 2 * MAXIMUM_LAG + 1

    blocks_first = jnp.transpose(strain_rate[0].reshape(piece, n_chan, channel_count), (1, 0, 2))
    gathered = lax.all_to_all(blocks_first, blocks_axis, 0, 0, tiled=True)
    receivers = normalize(gathered.reshape(n_chan * piece, channel_count), bandpass_taps)
    samples = receivers.shape[0]

    me = lax.axis_index("win")
    pick = (
        jnp.arange(channel_count, dtype=jnp.int32)[None, :]
        == spacing * jnp.arange(VIRTUAL_SOURCES, dtype=jnp.int32)[:, None]
    ).astype(receivers.dtype)
    sources = lax.dot_general(
        pick, receivers, (((1,), (1,)), ((), ())), preferred_element_type=jnp.float32
    ).astype(receivers.dtype).reshape(n_win, group, samples)
    source_pieces = [lax.dynamic_index_in_dim(sources, me, 0, keepdims=False)]
    receiver_pieces = [receivers]
    for distance in range(1, n_win):
        target = lax.rem(me + distance, n_win)
        source_pieces.append(
            shifted(lax.dynamic_index_in_dim(sources, target, 0, keepdims=False), "win", distance)
        )
        receiver_pieces.append(shifted(receivers, "win", distance))
    stack = jnp.stack(receiver_pieces)
    panel = jnp.stack(source_pieces)

    core = lax.axis_index("core")
    half = n_win // n_core
    share = panel.reshape(n_core, half, group, samples)
    mine = lax.dynamic_index_in_dim(share, core, 0, keepdims=False)
    other = lax.dynamic_index_in_dim(share, 1 - core, 0, keepdims=False)
    sibling = lax.ppermute(other, "core", [(0, 1), (1, 0)])
    first_is_mine = core == 0
    pair = jnp.stack([jnp.where(first_is_mine, mine, sibling), jnp.where(first_is_mine, sibling, mine)])
    own_half = lax.all_gather(pair, "chips", axis=0, tiled=True).reshape(n_chan, half, group, samples)
    other_half = lax.ppermute(own_half, "core", [(0, 1), (1, 0)])

    block = lax.axis_index("chips") * n_core + core
    offsets = pair_offsets[0]
    limits = lag_limit[0]
    slots = offsets.shape[0]
    partners = lax.rem(block + offsets + n_chan, n_chan)
    stack = stack.reshape(n_core, half, samples, channel_count)

    product = None
    for panels, which in ((own_half, core), (other_half, 1 - core)):
        if product is not None:
            panels, product = lax.optimization_barrier((panels, product))
        chosen = jnp.take(panels, partners, axis=0, mode="clip")
        padded = jnp.pad(chosen, ((0, 0), (0, 0), (0, 0), (MAXIMUM_LAG, MAXIMUM_LAG)))
        columns = []
        for w in range(half):
            lag_rows = jnp.stack([padded[:, w, :, i : i + samples] for i in range(lags)], axis=1)
            columns.append(lag_rows.reshape(slots * lags * group, samples))
        lagged = jnp.concatenate(columns, axis=1)
        partial = lax.dot_general(
            lagged,
            lax.dynamic_index_in_dim(stack, which, 0, keepdims=False).reshape(
                half * samples, channel_count
            ),
            (((1,), (0,)), ((), ())),
            preferred_element_type=jnp.float32,
        )
        product = partial if product is None else product + partial
    lag_ids = jnp.arange(lags, dtype=jnp.int32) - MAXIMUM_LAG
    kept = (jnp.abs(lag_ids)[None, :] <= limits[:, None]) & (offsets >= 0)[:, None]
    factor = 1.0 / math.sqrt(samples * n_win)
    weights = jnp.repeat(kept.astype(jnp.float32).reshape(slots * lags), group) * factor
    result = jnp.transpose(product * weights[:, None]).reshape(n_win, rows, slots * lags * group)
    result = lax.all_to_all(result, "win", 0, 0, tiled=True)
    result = result.reshape(n_win, rows, slots, lags, group)
    result = jnp.transpose(result, (2, 1, 3, 0, 4))
    return result.reshape(slots, rows, lags * VIRTUAL_SOURCES)


def solution(mesh):
    chan_size = mesh.shape["chan"]
    by_chip = Mesh(
        mesh.devices.reshape(chan_size // 2, 2, mesh.shape["win"]), ("chips", "core", "win")
    )
    blocks_axis = ("chips", "core")
    placed = (P("win", blocks_axis, None), P(), P(blocks_axis, None), P(blocks_axis, None))
    return jax.shard_map(
        on_device,
        mesh=by_chip,
        in_specs=placed,
        out_specs=P(None, ("chips", "core", "win"), None),
        check_vma=False,
    )
```

```python
import math

import jax
import jax.numpy as jnp
from jax import lax
from jax.sharding import Mesh, PartitionSpec as P


VIRTUAL_SOURCES = 128
MAXIMUM_LAG = 8


def shifted(block, axis, distance):
    devices = range(lax.axis_size(axis))
    route = [(i, (i + distance) % len(devices)) for i in devices]
    return lax.ppermute(block, axis, route)


def band_filter(values, taps):
    samples, channel_count = values.shape
    tap_count = taps.shape[0]
    half_width = (tap_count - 1) // 2
    block_len = min(256, samples)
    pieces = samples // block_len
    padded = jnp.pad(values, ((half_width, half_width), (0, 0)))
    head_rows = padded[:samples].reshape(pieces, block_len, channel_count)
    rest_rows = jnp.pad(padded[block_len:], ((0, block_len - 2 * half_width), (0, 0)))
    tail_rows = rest_rows.reshape(pieces, block_len, channel_count)[:, : 2 * half_width]
    window = jnp.concatenate([head_rows, tail_rows], axis=1)
    period = jnp.concatenate([taps, jnp.zeros((block_len,), taps.dtype)])
    matrix = jnp.tile(period, block_len)[: block_len * (block_len + 2 * half_width)]
    matrix = matrix.reshape(block_len, block_len + 2 * half_width)
    filtered = jnp.einsum("ij,bjc->bic", matrix, window, preferred_element_type=jnp.float32)
    return filtered.reshape(samples, channel_count)


def normalize(window, taps):
    filtered = band_filter(window, taps)
    tap_count = taps.shape[0]
    magnitude = jnp.abs(filtered).astype(jnp.bfloat16)
    box_taps = jnp.ones((tap_count,), jnp.bfloat16)
    mean_level = band_filter(magnitude, box_taps) * (1.0 / tap_count)
    return (filtered / (mean_level + 1e-05)).astype(jnp.bfloat16)


def on_device(strain_rate, bandpass_taps, pair_offsets, lag_limit):
    blocks_axis = ("chips", "core")
    n_chips = lax.axis_size("chips")
    n_core = lax.axis_size("core")
    n_chan = n_chips * n_core
    n_win = lax.axis_size("win")
    _, piece, channels = strain_rate.shape
    channel_count = channels // n_chan
    spacing = channel_count // VIRTUAL_SOURCES
    group = VIRTUAL_SOURCES // n_win
    rows = channel_count // n_win
    lags = 2 * MAXIMUM_LAG + 1

    blocks_first = jnp.transpose(strain_rate[0].reshape(piece, n_chan, channel_count), (1, 0, 2))
    gathered = lax.all_to_all(blocks_first, blocks_axis, 0, 0, tiled=True)
    receivers = normalize(gathered.reshape(n_chan * piece, channel_count), bandpass_taps)
    samples = receivers.shape[0]

    me = lax.axis_index("win")
    pick = (
        jnp.arange(channel_count, dtype=jnp.int32)[None, :]
        == spacing * jnp.arange(VIRTUAL_SOURCES, dtype=jnp.int32)[:, None]
    ).astype(receivers.dtype)
    sources = lax.dot_general(
        pick, receivers, (((1,), (1,)), ((), ())), preferred_element_type=jnp.float32
    ).astype(receivers.dtype).reshape(n_win, group, samples)
    source_pieces = [lax.dynamic_index_in_dim(sources, me, 0, keepdims=False)]
    for distance in range(1, n_win):
        target = lax.rem(me + distance, n_win)
        source_pieces.append(
            shifted(lax.dynamic_index_in_dim(sources, target, 0, keepdims=False), "win", distance)
        )
    stack = lax.all_gather(receivers, "win", axis=0, tiled=False)
    order = lax.rem(me - jnp.arange(n_win, dtype=jnp.int32) + n_win, n_win)
    panel = jnp.take(jnp.stack(source_pieces), order, axis=0, mode="clip")

    core = lax.axis_index("core")
    half = n_win // n_core
    share = panel.reshape(1, n_core, half, group, samples)
    share = jnp.broadcast_to(share, (n_chips, n_core, half, group, samples)).reshape(
        n_chan, half, group, samples
    )
    own_half = lax.all_to_all(share, blocks_axis, 0, 0, tiled=True)
    other_half = lax.ppermute(own_half, "core", [(0, 1), (1, 0)])

    block = lax.axis_index("chips") * n_core + core
    offsets = pair_offsets[0]
    limits = lag_limit[0]
    slots = offsets.shape[0]
    partners = lax.rem(block + offsets + n_chan, n_chan)
    stack = stack.reshape(n_core, half, samples, channel_count)

    product = None
    for panels, which in ((own_half, core), (other_half, 1 - core)):
        if product is not None:
            panels, product = lax.optimization_barrier((panels, product))
        chosen = jnp.take(panels, partners, axis=0, mode="clip")
        padded = jnp.pad(chosen, ((0, 0), (0, 0), (0, 0), (MAXIMUM_LAG, MAXIMUM_LAG)))
        columns = []
        for w in range(half):
            lag_rows = jnp.stack([padded[:, w, :, i : i + samples] for i in range(lags)], axis=1)
            columns.append(lag_rows.reshape(slots * lags * group, samples))
        lagged = jnp.concatenate(columns, axis=1)
        partial = lax.dot_general(
            lagged,
            lax.dynamic_index_in_dim(stack, which, 0, keepdims=False).reshape(
                half * samples, channel_count
            ),
            (((1,), (0,)), ((), ())),
            preferred_element_type=jnp.float32,
        )
        product = partial if product is None else product + partial
    lag_ids = jnp.arange(lags, dtype=jnp.int32) - MAXIMUM_LAG
    kept = (jnp.abs(lag_ids)[None, :] <= limits[:, None]) & (offsets >= 0)[:, None]
    factor = 1.0 / math.sqrt(samples * n_win)
    weights = jnp.repeat(kept.astype(jnp.float32).reshape(slots * lags), group) * factor
    result = jnp.transpose(product * weights[:, None]).reshape(n_win, rows, slots * lags * group)
    result = lax.all_to_all(result, "win", 0, 0, tiled=True)
    result = result.reshape(n_win, rows, slots, lags, group)
    result = jnp.transpose(result, (2, 1, 3, 0, 4))
    return result.reshape(slots, rows, lags * VIRTUAL_SOURCES)


def solution(mesh):
    chan_size = mesh.shape["chan"]
    by_chip = Mesh(
        mesh.devices.reshape(chan_size // 2, 2, mesh.shape["win"]), ("chips", "core", "win")
    )
    blocks_axis = ("chips", "core")
    placed = (P("win", blocks_axis, None), P(), P(blocks_axis, None), P(blocks_axis, None))
    return jax.shard_map(
        on_device,
        mesh=by_chip,
        in_specs=placed,
        out_specs=P(None, ("chips", "core", "win"), None),
        check_vma=False,
    )
```

```python
import math

import jax
import jax.numpy as jnp
from jax import lax
from jax.sharding import Mesh, PartitionSpec as P


VIRTUAL_SOURCES = 128
MAXIMUM_LAG = 8


def shifted(block, axis, distance):
    devices = range(lax.axis_size(axis))
    route = [(i, (i + distance) % len(devices)) for i in devices]
    return lax.ppermute(block, axis, route)


def band_filter(values, taps):
    samples, channel_count = values.shape
    tap_count = taps.shape[0]
    half_width = (tap_count - 1) // 2
    block_len = min(256, samples)
    pieces = samples // block_len
    padded = jnp.pad(values, ((half_width, half_width), (0, 0)))
    head_rows = padded[:samples].reshape(pieces, block_len, channel_count)
    rest_rows = jnp.pad(padded[block_len:], ((0, block_len - 2 * half_width), (0, 0)))
    tail_rows = rest_rows.reshape(pieces, block_len, channel_count)[:, : 2 * half_width]
    window = jnp.concatenate([head_rows, tail_rows], axis=1)
    period = jnp.concatenate([taps, jnp.zeros((block_len,), taps.dtype)])
    matrix = jnp.tile(period, block_len)[: block_len * (block_len + 2 * half_width)]
    matrix = matrix.reshape(block_len, block_len + 2 * half_width)
    filtered = jnp.einsum("ij,bjc->bic", matrix, window, preferred_element_type=jnp.float32)
    return filtered.reshape(samples, channel_count)


def normalize(window, taps):
    filtered = band_filter(window, taps)
    tap_count = taps.shape[0]
    magnitude = jnp.abs(filtered).astype(jnp.bfloat16)
    box_taps = jnp.ones((tap_count,), jnp.bfloat16)
    mean_level = band_filter(magnitude, box_taps) * (1.0 / tap_count)
    return (filtered / (mean_level + 1e-05)).astype(jnp.bfloat16)


def on_device(strain_rate, bandpass_taps, pair_offsets, lag_limit):
    blocks_axis = ("chips", "core")
    n_chips = lax.axis_size("chips")
    n_core = lax.axis_size("core")
    n_chan = n_chips * n_core
    n_win = lax.axis_size("win")
    _, piece, channels = strain_rate.shape
    channel_count = channels // n_chan
    spacing = channel_count // VIRTUAL_SOURCES
    group = VIRTUAL_SOURCES // n_win
    rows = channel_count // n_win
    lags = 2 * MAXIMUM_LAG + 1

    blocks_first = jnp.transpose(strain_rate[0].reshape(piece, n_chan, channel_count), (1, 0, 2))
    gathered = lax.all_to_all(blocks_first, blocks_axis, 0, 0, tiled=True)
    receivers = normalize(gathered.reshape(n_chan * piece, channel_count), bandpass_taps)
    samples = receivers.shape[0]

    me = lax.axis_index("win")
    pick = (
        jnp.arange(channel_count, dtype=jnp.int32)[None, :]
        == spacing * jnp.arange(VIRTUAL_SOURCES, dtype=jnp.int32)[:, None]
    ).astype(receivers.dtype)
    sources = lax.dot_general(
        pick, receivers, (((1,), (1,)), ((), ())), preferred_element_type=jnp.float32
    ).astype(receivers.dtype).reshape(n_win, group, samples)
    source_pieces = [lax.dynamic_index_in_dim(sources, me, 0, keepdims=False)]
    receiver_pieces = [receivers]
    for distance in range(1, n_win):
        target = lax.rem(me + distance, n_win)
        source_pieces.append(
            shifted(lax.dynamic_index_in_dim(sources, target, 0, keepdims=False), "win", distance)
        )
        receiver_pieces.append(shifted(receivers, "win", distance))
    stack = jnp.stack(receiver_pieces)
    panel = jnp.stack(source_pieces)

    core = lax.axis_index("core")
    half = n_win // n_core
    share = panel.reshape(1, n_core, half, group, samples)
    share = jnp.broadcast_to(share, (n_chips, n_core, half, group, samples)).reshape(
        n_chan, half, group, samples
    )
    own_half = lax.all_to_all(share, blocks_axis, 0, 0, tiled=True)
    other_half = lax.ppermute(own_half, "core", [(0, 1), (1, 0)])

    block = lax.axis_index("chips") * n_core + core
    offsets = pair_offsets[0]
    limits = lag_limit[0]
    slots = offsets.shape[0]
    partners = lax.rem(block + offsets + n_chan, n_chan)
    stack = stack.reshape(n_core, half, samples, channel_count)

    product = None
    for panels, which in ((own_half, core), (other_half, 1 - core)):
        if product is not None:
            panels, product = lax.optimization_barrier((panels, product))
        chosen = jnp.take(panels, partners, axis=0, mode="clip")
        padded = jnp.pad(chosen, ((0, 0), (0, 0), (0, 0), (MAXIMUM_LAG, MAXIMUM_LAG)))
        columns = []
        for w in range(half):
            lag_rows = jnp.stack([padded[:, w, :, i : i + samples] for i in range(lags)], axis=1)
            columns.append(lag_rows.reshape(slots * lags * group, samples))
        lagged = jnp.concatenate(columns, axis=1)
        partial = lax.dot_general(
            lagged,
            lax.dynamic_index_in_dim(stack, which, 0, keepdims=False).reshape(
                half * samples, channel_count
            ),
            (((1,), (0,)), ((), ())),
            preferred_element_type=jnp.float32,
        )
        product = partial if product is None else product + partial
    lag_ids = jnp.arange(lags, dtype=jnp.int32) - MAXIMUM_LAG
    kept = (jnp.abs(lag_ids)[None, :] <= limits[:, None]) & (offsets >= 0)[:, None]
    factor = 1.0 / math.sqrt(samples * n_win)
    weights = jnp.repeat(kept.astype(jnp.float32).reshape(slots * lags), group) * factor
    result = jnp.transpose(product * weights[:, None]).reshape(n_win, rows, slots * lags * group)
    result = lax.all_to_all(result, "win", 0, 0, tiled=True)
    result = result.reshape(n_win, rows, slots, lags, group)
    result = jnp.transpose(result, (2, 1, 3, 0, 4))
    return result.reshape(slots, rows, lags * VIRTUAL_SOURCES)


def solution(mesh):
    chan_size = mesh.shape["chan"]
    by_chip = Mesh(
        mesh.devices.reshape(chan_size // 2, 2, mesh.shape["win"]), ("chips", "core", "win")
    )
    blocks_axis = ("chips", "core")
    placed = (P("win", blocks_axis, None), P(), P(blocks_axis, None), P(blocks_axis, None))
    return jax.shard_map(
        on_device,
        mesh=by_chip,
        in_specs=placed,
        out_specs=P(None, ("chips", "core", "win"), None),
        check_vma=False,
    )
```

```python
import math

import jax
import jax.numpy as jnp
from jax import lax
from jax.sharding import Mesh, PartitionSpec as P


VIRTUAL_SOURCES = 128
MAXIMUM_LAG = 8


def shifted(block, axis, distance):
    devices = range(lax.axis_size(axis))
    route = [(i, (i + distance) % len(devices)) for i in devices]
    return lax.ppermute(block, axis, route)


def band_filter(values, taps):
    samples, channel_count = values.shape
    tap_count = taps.shape[0]
    half_width = (tap_count - 1) // 2
    block_len = min(256, samples)
    pieces = samples // block_len
    padded = jnp.pad(values, ((half_width, half_width), (0, 0)))
    head_rows = padded[:samples].reshape(pieces, block_len, channel_count)
    rest_rows = jnp.pad(padded[block_len:], ((0, block_len - 2 * half_width), (0, 0)))
    tail_rows = rest_rows.reshape(pieces, block_len, channel_count)[:, : 2 * half_width]
    window = jnp.concatenate([head_rows, tail_rows], axis=1)
    period = jnp.concatenate([taps, jnp.zeros((block_len,), taps.dtype)])
    matrix = jnp.tile(period, block_len)[: block_len * (block_len + 2 * half_width)]
    matrix = matrix.reshape(block_len, block_len + 2 * half_width)
    filtered = jnp.einsum("ij,bjc->bic", matrix, window, preferred_element_type=jnp.float32)
    return filtered.reshape(samples, channel_count)


def normalize(window, taps):
    filtered = band_filter(window, taps)
    tap_count = taps.shape[0]
    magnitude = jnp.abs(filtered).astype(jnp.bfloat16)
    box_taps = jnp.ones((tap_count,), jnp.bfloat16)
    mean_level = band_filter(magnitude, box_taps) * (1.0 / tap_count)
    return (filtered / (mean_level + 1e-05)).astype(jnp.bfloat16)


def on_device(strain_rate, bandpass_taps, pair_offsets, lag_limit):
    blocks_axis = ("chips", "core")
    n_chips = lax.axis_size("chips")
    n_core = lax.axis_size("core")
    n_chan = n_chips * n_core
    n_win = lax.axis_size("win")
    _, piece, channels = strain_rate.shape
    channel_count = channels // n_chan
    spacing = channel_count // VIRTUAL_SOURCES
    group = VIRTUAL_SOURCES // n_win
    rows = channel_count // n_win
    lags = 2 * MAXIMUM_LAG + 1

    blocks_first = jnp.transpose(strain_rate[0].reshape(piece, n_chan, channel_count), (1, 0, 2))
    gathered = lax.all_to_all(blocks_first, blocks_axis, 0, 0, tiled=True)
    receivers = normalize(gathered.reshape(n_chan * piece, channel_count), bandpass_taps)
    samples = receivers.shape[0]

    me = lax.axis_index("win")
    pick = (
        jnp.arange(channel_count, dtype=jnp.int32)[None, :]
        == spacing * jnp.arange(VIRTUAL_SOURCES, dtype=jnp.int32)[:, None]
    ).astype(receivers.dtype)
    sources = lax.dot_general(
        pick, receivers, (((1,), (1,)), ((), ())), preferred_element_type=jnp.float32
    ).astype(receivers.dtype).reshape(n_win, group, samples)
    source_pieces = [lax.dynamic_index_in_dim(sources, me, 0, keepdims=False)]
    receiver_pieces = [receivers]
    for distance in range(1, n_win):
        target = lax.rem(me + distance, n_win)
        source_pieces.append(
            shifted(lax.dynamic_index_in_dim(sources, target, 0, keepdims=False), "win", distance)
        )

    ring = n_win // 2
    x_part = me // ring
    y_part = me % ring
    for distance in range(1, ring):
        route = [(i, (i // ring) * ring + (i % ring + distance) % ring) for i in range(n_win)]
        receiver_pieces.append(lax.ppermute(receivers, "win", route))
    near = jnp.stack(receiver_pieces)
    far = lax.ppermute(near, "win", [(i, (i + ring) % n_win) for i in range(n_win)])
    stack = jnp.concatenate([near, far])
    position = jnp.arange(n_win, dtype=jnp.int32)
    window_of = ((x_part + position // ring) % 2) * ring + (y_part - position % ring + ring) % ring
    piece_of = lax.rem(me - window_of + n_win, n_win)
    panel = jnp.take(jnp.stack(source_pieces), piece_of, axis=0, mode="clip")

    core = lax.axis_index("core")
    half = n_win // n_core
    share = panel.reshape(1, n_core, half, group, samples)
    share = jnp.broadcast_to(share, (n_chips, n_core, half, group, samples)).reshape(
        n_chan, half, group, samples
    )
    own_half = lax.all_to_all(share, blocks_axis, 0, 0, tiled=True)
    other_half = lax.ppermute(own_half, "core", [(0, 1), (1, 0)])

    block = lax.axis_index("chips") * n_core + core
    offsets = pair_offsets[0]
    limits = lag_limit[0]
    slots = offsets.shape[0]
    partners = lax.rem(block + offsets + n_chan, n_chan)
    stack = stack.reshape(n_core, half, samples, channel_count)

    product = None
    for panels, which in ((own_half, core), (other_half, 1 - core)):
        if product is not None:
            panels, product = lax.optimization_barrier((panels, product))
        chosen = jnp.take(panels, partners, axis=0, mode="clip")
        padded = jnp.pad(chosen, ((0, 0), (0, 0), (0, 0), (MAXIMUM_LAG, MAXIMUM_LAG)))
        columns = []
        for w in range(half):
            lag_rows = jnp.stack([padded[:, w, :, i : i + samples] for i in range(lags)], axis=1)
            columns.append(lag_rows.reshape(slots * lags * group, samples))
        lagged = jnp.concatenate(columns, axis=1)
        partial = lax.dot_general(
            lagged,
            lax.dynamic_index_in_dim(stack, which, 0, keepdims=False).reshape(
                half * samples, channel_count
            ),
            (((1,), (0,)), ((), ())),
            preferred_element_type=jnp.float32,
        )
        product = partial if product is None else product + partial
    lag_ids = jnp.arange(lags, dtype=jnp.int32) - MAXIMUM_LAG
    kept = (jnp.abs(lag_ids)[None, :] <= limits[:, None]) & (offsets >= 0)[:, None]
    factor = 1.0 / math.sqrt(samples * n_win)
    weights = jnp.repeat(kept.astype(jnp.float32).reshape(slots * lags), group) * factor
    result = jnp.transpose(product * weights[:, None]).reshape(n_win, rows, slots * lags * group)
    result = lax.all_to_all(result, "win", 0, 0, tiled=True)
    result = result.reshape(n_win, rows, slots, lags, group)
    result = jnp.transpose(result, (2, 1, 3, 0, 4))
    return result.reshape(slots, rows, lags * VIRTUAL_SOURCES)


def solution(mesh):
    chan_size = mesh.shape["chan"]
    by_chip = Mesh(
        mesh.devices.reshape(chan_size // 2, 2, mesh.shape["win"]), ("chips", "core", "win")
    )
    blocks_axis = ("chips", "core")
    placed = (P("win", blocks_axis, None), P(), P(blocks_axis, None), P(blocks_axis, None))
    return jax.shard_map(
        on_device,
        mesh=by_chip,
        in_specs=placed,
        out_specs=P(None, ("chips", "core", "win"), None),
        check_vma=False,
    )
```

```python
import math

import jax
import jax.numpy as jnp
from jax import lax
from jax.sharding import Mesh, PartitionSpec as P


VIRTUAL_SOURCES = 128
MAXIMUM_LAG = 8


def shifted(block, axis, distance):
    devices = range(lax.axis_size(axis))
    route = [(i, (i + distance) % len(devices)) for i in devices]
    return lax.ppermute(block, axis, route)


def band_filter(values, taps):
    samples, channel_count = values.shape
    tap_count = taps.shape[0]
    half_width = (tap_count - 1) // 2
    block_len = min(256, samples)
    pieces = samples // block_len
    padded = jnp.pad(values, ((half_width, half_width), (0, 0)))
    head_rows = padded[:samples].reshape(pieces, block_len, channel_count)
    rest_rows = jnp.pad(padded[block_len:], ((0, block_len - 2 * half_width), (0, 0)))
    tail_rows = rest_rows.reshape(pieces, block_len, channel_count)[:, : 2 * half_width]
    window = jnp.concatenate([head_rows, tail_rows], axis=1)
    period = jnp.concatenate([taps, jnp.zeros((block_len,), taps.dtype)])
    matrix = jnp.tile(period, block_len)[: block_len * (block_len + 2 * half_width)]
    matrix = matrix.reshape(block_len, block_len + 2 * half_width)
    filtered = jnp.einsum("ij,bjc->bic", matrix, window, preferred_element_type=jnp.float32)
    return filtered.reshape(samples, channel_count)


def normalize(window, taps):
    filtered = band_filter(window, taps)
    tap_count = taps.shape[0]
    magnitude = jnp.abs(filtered).astype(jnp.bfloat16)
    box_taps = jnp.ones((tap_count,), jnp.bfloat16)
    mean_level = band_filter(magnitude, box_taps) * (1.0 / tap_count)
    return (filtered / (mean_level + 1e-05)).astype(jnp.bfloat16)


def on_device(strain_rate, bandpass_taps, pair_offsets, lag_limit):
    blocks_axis = ("chips", "core")
    n_chips = lax.axis_size("chips")
    n_core = lax.axis_size("core")
    n_chan = n_chips * n_core
    n_win = lax.axis_size("win")
    _, piece, channels = strain_rate.shape
    channel_count = channels // n_chan
    spacing = channel_count // VIRTUAL_SOURCES
    group = VIRTUAL_SOURCES // n_win
    rows = channel_count // n_win
    lags = 2 * MAXIMUM_LAG + 1

    blocks_first = jnp.transpose(strain_rate[0].reshape(piece, n_chan, channel_count), (1, 0, 2))
    gathered = lax.all_to_all(blocks_first, blocks_axis, 0, 0, tiled=True)
    receivers = normalize(gathered.reshape(n_chan * piece, channel_count), bandpass_taps)
    samples = receivers.shape[0]

    me = lax.axis_index("win")
    pick = (
        jnp.arange(channel_count, dtype=jnp.int32)[None, :]
        == spacing * jnp.arange(VIRTUAL_SOURCES, dtype=jnp.int32)[:, None]
    ).astype(receivers.dtype)
    sources = lax.dot_general(
        pick, receivers, (((1,), (1,)), ((), ())), preferred_element_type=jnp.float32
    ).astype(receivers.dtype).reshape(n_win, group, samples)
    source_pieces = [lax.dynamic_index_in_dim(sources, me, 0, keepdims=False)]
    receiver_pieces = [receivers]
    for distance in range(1, n_win):
        target = lax.rem(me + distance, n_win)
        source_pieces.append(
            shifted(lax.dynamic_index_in_dim(sources, target, 0, keepdims=False), "win", distance)
        )

    ring = n_win // 2
    x_part = me // ring
    y_part = me % ring
    for distance in range(1, ring):
        route = [(i, (i // ring) * ring + (i % ring + distance) % ring) for i in range(n_win)]
        receiver_pieces.append(lax.ppermute(receivers, "win", route))
    flip = [(i, (i + ring) % n_win) for i in range(n_win)]
    far_pieces = [lax.ppermute(one, "win", flip) for one in receiver_pieces]
    stack = jnp.stack(receiver_pieces + far_pieces)
    position = jnp.arange(n_win, dtype=jnp.int32)
    window_of = ((x_part + position // ring) % 2) * ring + (y_part - position % ring + ring) % ring
    piece_of = lax.rem(me - window_of + n_win, n_win)
    panel = jnp.take(jnp.stack(source_pieces), piece_of, axis=0, mode="clip")

    core = lax.axis_index("core")
    half = n_win // n_core
    share = panel.reshape(1, n_core, half, group, samples)
    share = jnp.broadcast_to(share, (n_chips, n_core, half, group, samples)).reshape(
        n_chan, half, group, samples
    )
    own_half = lax.all_to_all(share, blocks_axis, 0, 0, tiled=True)
    other_half = lax.ppermute(own_half, "core", [(0, 1), (1, 0)])

    block = lax.axis_index("chips") * n_core + core
    offsets = pair_offsets[0]
    limits = lag_limit[0]
    slots = offsets.shape[0]
    partners = lax.rem(block + offsets + n_chan, n_chan)
    stack = stack.reshape(n_core, half, samples, channel_count)

    product = None
    for panels, which in ((own_half, core), (other_half, 1 - core)):
        if product is not None:
            panels, product = lax.optimization_barrier((panels, product))
        chosen = jnp.take(panels, partners, axis=0, mode="clip")
        padded = jnp.pad(chosen, ((0, 0), (0, 0), (0, 0), (MAXIMUM_LAG, MAXIMUM_LAG)))
        columns = []
        for w in range(half):
            lag_rows = jnp.stack([padded[:, w, :, i : i + samples] for i in range(lags)], axis=1)
            columns.append(lag_rows.reshape(slots * lags * group, samples))
        lagged = jnp.concatenate(columns, axis=1)
        partial = lax.dot_general(
            lagged,
            lax.dynamic_index_in_dim(stack, which, 0, keepdims=False).reshape(
                half * samples, channel_count
            ),
            (((1,), (0,)), ((), ())),
            preferred_element_type=jnp.float32,
        )
        product = partial if product is None else product + partial
    lag_ids = jnp.arange(lags, dtype=jnp.int32) - MAXIMUM_LAG
    kept = (jnp.abs(lag_ids)[None, :] <= limits[:, None]) & (offsets >= 0)[:, None]
    factor = 1.0 / math.sqrt(samples * n_win)
    weights = jnp.repeat(kept.astype(jnp.float32).reshape(slots * lags), group) * factor
    result = jnp.transpose(product * weights[:, None]).reshape(n_win, rows, slots * lags * group)
    result = lax.all_to_all(result, "win", 0, 0, tiled=True)
    result = result.reshape(n_win, rows, slots, lags, group)
    result = jnp.transpose(result, (2, 1, 3, 0, 4))
    return result.reshape(slots, rows, lags * VIRTUAL_SOURCES)


def solution(mesh):
    chan_size = mesh.shape["chan"]
    by_chip = Mesh(
        mesh.devices.reshape(chan_size // 2, 2, mesh.shape["win"]), ("chips", "core", "win")
    )
    blocks_axis = ("chips", "core")
    placed = (P("win", blocks_axis, None), P(), P(blocks_axis, None), P(blocks_axis, None))
    return jax.shard_map(
        on_device,
        mesh=by_chip,
        in_specs=placed,
        out_specs=P(None, ("chips", "core", "win"), None),
        check_vma=False,
    )
```

```python
import math

import jax
import jax.numpy as jnp
from jax import lax
from jax.sharding import Mesh, PartitionSpec as P


VIRTUAL_SOURCES = 128
MAXIMUM_LAG = 8


def band_filter(values, taps):
    samples, channel_count = values.shape
    tap_count = taps.shape[0]
    half_width = (tap_count - 1) // 2
    block_len = min(256, samples)
    pieces = samples // block_len
    padded = jnp.pad(values, ((half_width, half_width), (0, 0)))
    head_rows = padded[:samples].reshape(pieces, block_len, channel_count)
    rest_rows = jnp.pad(padded[block_len:], ((0, block_len - 2 * half_width), (0, 0)))
    tail_rows = rest_rows.reshape(pieces, block_len, channel_count)[:, : 2 * half_width]
    window = jnp.concatenate([head_rows, tail_rows], axis=1)
    period = jnp.concatenate([taps, jnp.zeros((block_len,), taps.dtype)])
    matrix = jnp.tile(period, block_len)[: block_len * (block_len + 2 * half_width)]
    matrix = matrix.reshape(block_len, block_len + 2 * half_width)
    filtered = jnp.einsum("ij,bjc->bic", matrix, window, preferred_element_type=jnp.float32)
    return filtered.reshape(samples, channel_count)


def normalize(window, taps):
    filtered = band_filter(window, taps)
    tap_count = taps.shape[0]
    magnitude = jnp.abs(filtered).astype(jnp.bfloat16)
    box_taps = jnp.ones((tap_count,), jnp.bfloat16)
    mean_level = band_filter(magnitude, box_taps) * (1.0 / tap_count)
    return (filtered / (mean_level + 1e-05)).astype(jnp.bfloat16)


def on_device(strain_rate, bandpass_taps, pair_offsets, lag_limit):
    blocks_axis = ("chips", "core")
    n_chips = lax.axis_size("chips")
    n_core = lax.axis_size("core")
    n_chan = n_chips * n_core
    n_win = lax.axis_size("win")
    _, piece, channels = strain_rate.shape
    channel_count = channels // n_chan
    spacing = channel_count // VIRTUAL_SOURCES
    group = VIRTUAL_SOURCES // n_win
    rows = channel_count // n_win
    lags = 2 * MAXIMUM_LAG + 1

    blocks_first = jnp.transpose(strain_rate[0].reshape(piece, n_chan, channel_count), (1, 0, 2))
    gathered = lax.all_to_all(blocks_first, blocks_axis, 0, 0, tiled=True)
    receivers = normalize(gathered.reshape(n_chan * piece, channel_count), bandpass_taps)
    samples = receivers.shape[0]

    me = lax.axis_index("win")
    pick = (
        jnp.arange(channel_count, dtype=jnp.int32)[None, :]
        == spacing * jnp.arange(VIRTUAL_SOURCES, dtype=jnp.int32)[:, None]
    ).astype(receivers.dtype)
    sources = lax.dot_general(
        pick, receivers, (((1,), (1,)), ((), ())), preferred_element_type=jnp.float32
    ).astype(receivers.dtype).reshape(n_win, group, samples)
    sources = lax.all_to_all(sources, "win", 0, 0, tiled=True)
    receiver_pieces = [receivers]

    ring = n_win // 2
    x_part = me // ring
    y_part = me % ring
    for distance in range(1, ring):
        route = [(i, (i // ring) * ring + (i % ring + distance) % ring) for i in range(n_win)]
        receiver_pieces.append(lax.ppermute(receivers, "win", route))
    flip = [(i, (i + ring) % n_win) for i in range(n_win)]
    far_pieces = [lax.ppermute(one, "win", flip) for one in receiver_pieces]
    stack = jnp.stack(receiver_pieces + far_pieces)
    position = jnp.arange(n_win, dtype=jnp.int32)
    window_of = ((x_part + position // ring) % 2) * ring + (y_part - position % ring + ring) % ring
    panel = jnp.take(sources, window_of, axis=0, mode="clip")

    core = lax.axis_index("core")
    half = n_win // n_core
    share = panel.reshape(1, n_core, half, group, samples)
    share = jnp.broadcast_to(share, (n_chips, n_core, half, group, samples)).reshape(
        n_chan, half, group, samples
    )
    own_half = lax.all_to_all(share, blocks_axis, 0, 0, tiled=True)
    other_half = lax.ppermute(own_half, "core", [(0, 1), (1, 0)])

    block = lax.axis_index("chips") * n_core + core
    offsets = pair_offsets[0]
    limits = lag_limit[0]
    slots = offsets.shape[0]
    partners = lax.rem(block + offsets + n_chan, n_chan)
    stack = stack.reshape(n_core, half, samples, channel_count)

    product = None
    for panels, which in ((own_half, core), (other_half, 1 - core)):
        if product is not None:
            panels, product = lax.optimization_barrier((panels, product))
        chosen = jnp.take(panels, partners, axis=0, mode="clip")
        padded = jnp.pad(chosen, ((0, 0), (0, 0), (0, 0), (MAXIMUM_LAG, MAXIMUM_LAG)))
        columns = []
        for w in range(half):
            lag_rows = jnp.stack([padded[:, w, :, i : i + samples] for i in range(lags)], axis=1)
            columns.append(lag_rows.reshape(slots * lags * group, samples))
        lagged = jnp.concatenate(columns, axis=1)
        partial = lax.dot_general(
            lagged,
            lax.dynamic_index_in_dim(stack, which, 0, keepdims=False).reshape(
                half * samples, channel_count
            ),
            (((1,), (0,)), ((), ())),
            preferred_element_type=jnp.float32,
        )
        product = partial if product is None else product + partial
    lag_ids = jnp.arange(lags, dtype=jnp.int32) - MAXIMUM_LAG
    kept = (jnp.abs(lag_ids)[None, :] <= limits[:, None]) & (offsets >= 0)[:, None]
    factor = 1.0 / math.sqrt(samples * n_win)
    weights = jnp.repeat(kept.astype(jnp.float32).reshape(slots * lags), group) * factor
    result = jnp.transpose(product * weights[:, None]).reshape(n_win, rows, slots * lags * group)
    result = lax.all_to_all(result, "win", 0, 0, tiled=True)
    result = result.reshape(n_win, rows, slots, lags, group)
    result = jnp.transpose(result, (2, 1, 3, 0, 4))
    return result.reshape(slots, rows, lags * VIRTUAL_SOURCES)


def solution(mesh):
    chan_size = mesh.shape["chan"]
    by_chip = Mesh(
        mesh.devices.reshape(chan_size // 2, 2, mesh.shape["win"]), ("chips", "core", "win")
    )
    blocks_axis = ("chips", "core")
    placed = (P("win", blocks_axis, None), P(), P(blocks_axis, None), P(blocks_axis, None))
    return jax.shard_map(
        on_device,
        mesh=by_chip,
        in_specs=placed,
        out_specs=P(None, ("chips", "core", "win"), None),
        check_vma=False,
    )
```
